512 devices in a mesh: dp: 8 (over x, core), tensor: 64 (over z, y).
Axes of the slice: x: 4, y: 4, z: 16, core: 2. Of those that a mesh axis runs over, the one named last changes fastest.
Arguments:
- states: bfloat16 [65536, 2048], P(('dp', 'tensor')), may hold values from -150 to 150
- norm_gain: float32 [2048], replicated, may hold values from 0.1 to 1.9
- norm_bias: float32 [2048], replicated, may hold values from -3 to 3
- head_table: bfloat16 [250880, 2048], P('tensor', 'dp'), may hold values from -2 to 2
- seq_lengths: int32 [8], P('dp'), may hold values from 4096 to 8192
- scored_index: int32 [2048], P('dp'), may hold values from 0 to 8191
- targets: int32 [2048], P('dp'), may hold values from 0 to 250879
- slot_mask: int32 [2048], P('dp'), may hold values 0 or 1
Outputs:
- logprob: float32 [2048], P(('dp', 'tensor'))
- entropy: float32 [2048], P(('dp', 'tensor'))
The draws below stay inside these ranges and needn't reach their ends.
All inputs are finite; a program needn't handle non-finite values. No bound on the sum of `slot_mask` on one device may be relied on, other than what follows from the above.
Results may differ from the reference program's by a relative error of at most 0.012.
The reference program's roundings to bfloat16 on the way (of `normed` and `chosen`) count: a program that leaves them out, or rounds other values in their place, can miss the bound.
Values may be sent and summed in bfloat16 or wider, within the bound.
No kernel may reach another device: no remote copies, remote signals or barrier semaphores. Data moves between devices by JAX's collectives and lax.ppermute only.
A program may use at most 64 MiB of HBM per device.

```python
import math
import jax
import jax.numpy as jnp
import numpy as np
from jax import lax

D = 2048
VOCAB = 250880
SCORED_DP = 256
SEQS_DP = 1
POS_DP = 8192
POSITIONS = 65536
SCORED = 2048
NSEQ = 8
N_DP = 8


def shared_plan(key):
    scored = jax.random.randint(jax.random.fold_in(key, 103), (SCORED,), 0, POS_DP)
    scored = scored.at[0].set(0).at[SCORED - 1].set(POS_DP - 1)
    return scored


def draw_scored_index(key, part):
    return shared_plan(key).astype(jnp.int32)


def draw_states(key, part):
    base = jnp.clip(jax.random.normal(jax.random.fold_in(key, 1), (POSITIONS, D), jnp.float32), -5.0, 5.0)
    row_scale = jnp.exp(jax.random.uniform(jax.random.fold_in(key, 2), (POSITIONS, 1), jnp.float32, 0.0, math.log(10.0)))
    col_scale = 0.3 * jnp.exp(jax.random.uniform(jax.random.fold_in(key, 3), (1, D), jnp.float32, 0.0, math.log(10.0)))
    values = base * row_scale * col_scale
    return values.astype(jnp.bfloat16)


def draw_head_table(key, part):
    base = jnp.clip(jax.random.normal(jax.random.fold_in(key, 11), (VOCAB, D), jnp.float32), -5.5, 5.5)
    rising = 1.0 + jnp.arange(VOCAB, dtype=jnp.float32) / VOCAB
    spread = jnp.exp(jax.random.uniform(jax.random.fold_in(key, 12), (VOCAB,), jnp.float32, 0.0, math.log(10.0)))
    values = base * (spread * rising * (0.7 / math.sqrt(D)))[:, None]
    return values.astype(jnp.bfloat16)


def place_ends(array, key, least, high):
    spot = [jax.random.randint(jax.random.fold_in(key, axis), (), 0, length) for axis, length in enumerate(array.shape)]
    longest = array.shape.index(max(array.shape))
    beside = spot[:longest] + [(spot[longest] + 1) % array.shape[longest]] + spot[longest + 1:]
    return array.at[tuple(spot)].set(least).at[tuple(beside)].set(high)


def ranked_wide(rng, dims, number_of, lean):
    loads = [min(1 << octave, number_of + 1 - (1 << octave)) * (1 << 20) // math.isqrt((1 << octave) ** lean) + 1 for octave in range((number_of + 1).bit_length()) if 1 << octave <= number_of]
    width = 1 + sum(loads) // (1 << 30)
    table = np.cumsum(np.array([max(1, weight // width) for weight in loads]))
    ticket = jax.random.randint(jax.random.fold_in(rng, 1), dims, 0, int(table[len(loads) - 1]))
    start = jnp.left_shift(1, jnp.searchsorted(jnp.asarray(table, jnp.int32), ticket, side="right").astype(jnp.int32))
    grade = start - 1 + jax.random.randint(jax.random.fold_in(rng, 4), dims, 0, 1 << 30) % jnp.minimum(start, number_of + 1 - start)
    return jax.random.permutation(jax.random.fold_in(rng, 2), number_of)[grade].astype(jnp.int32)


def gaussian(rng, dims, width, most, kind=jnp.bfloat16):
    result = width * jax.random.normal(rng, dims, jnp.float32)
    return jnp.clip(result, min=-most, max=most).astype(kind)


def setup_inputs(seed: int = 0) -> dict:
    keys = jax.random.split(jax.random.key(seed), 9)
    states = draw_states(jax.random.fold_in(keys[8], 71), 0)
    norm_gain = jnp.clip(1.0 + 0.18 * jax.random.normal(keys[1], (D,), jnp.float32), 0.1, 1.9)
    norm_bias = gaussian(keys[2], (D,), 0.5, 3.0, jnp.float32)
    head_table = draw_head_table(jax.random.fold_in(keys[8], 71), 0)
    seq_lengths = place_ends(jax.random.randint(keys[4], (NSEQ,), POS_DP // SEQS_DP // 2, POS_DP // SEQS_DP + 1), jax.random.fold_in(keys[4], 1), POS_DP // SEQS_DP // 2, (POS_DP // SEQS_DP + 1) - 1).astype(jnp.int32)
    scored_index = draw_scored_index(jax.random.fold_in(keys[8], 71), 0)
    targets = place_ends(ranked_wide(keys[6], (SCORED,), VOCAB, 2), jax.random.fold_in(keys[6], 3), 0, VOCAB - 1).astype(jnp.int32)
    slot_mask = place_ends((jax.random.randint(keys[7], (SCORED,), 0, 4) < 3).astype(jnp.int32), jax.random.fold_in(keys[7], 1), 0, 1)
    return {"states": states, "norm_gain": norm_gain, "norm_bias": norm_bias, "head_table": head_table, "seq_lengths": seq_lengths, "scored_index": scored_index, "targets": targets, "slot_mask": slot_mask}


EPSILON = 1e-05

def layer_norm(states, norm_gain, norm_bias):
    values = states.astype(jnp.float32)
    center = lax.optimization_barrier(jnp.mean(values, axis=1, keepdims=True))
    shifted = values - center
    variance = lax.optimization_barrier(jnp.mean(shifted * shifted, axis=1, keepdims=True))
    return (shifted * lax.rsqrt(variance + EPSILON) * norm_gain + norm_bias).astype(jnp.bfloat16)

def reference(states, norm_gain, norm_bias, head_table, seq_lengths, scored_index, targets, slot_mask):
    normed = layer_norm(states, norm_gain, norm_bias)
    grouped = normed.reshape(N_DP, POS_DP, D)
    index_groups = scored_index.reshape(N_DP, SCORED_DP)
    target_groups = targets.reshape(N_DP, SCORED_DP)

    def one_group(inputs):
        rows_group, index_group, target_group = inputs
        chosen = jnp.take(rows_group, index_group, axis=0)
        logits = lax.dot_general(chosen, head_table, (((1,), (1,)), ((), ())), preferred_element_type=jnp.float32)
        maxima = lax.optimization_barrier(jnp.max(logits, axis=1))
        shifted = logits - maxima[:, None]
        weights = jnp.exp(shifted)
        totals = lax.optimization_barrier(jnp.sum(weights, axis=1))
        weighted = lax.optimization_barrier(jnp.sum(weights * shifted, axis=1))
        target_logit = jnp.take_along_axis(logits, target_group[:, None], axis=1)[:, 0]
        log_total = jnp.log(totals)
        return (target_logit - maxima - log_total, log_total - weighted / totals)
    logprob, entropy = lax.map(one_group, (grouped, index_groups, target_groups))
    logprob = logprob.reshape(SCORED)
    entropy = entropy.reshape(SCORED)
    segment = POS_DP // SEQS_DP
    group_of = jnp.arange(SCORED, dtype=jnp.int32) // SCORED_DP
    seq_global = (group_of * SEQS_DP + scored_index // segment).astype(jnp.int32)
    length_of = jnp.take(seq_lengths, seq_global, axis=0)
    live = (slot_mask == 1) & (scored_index % segment < length_of)
    return (jnp.where(live, logprob, 0.0), jnp.where(live, entropy, 0.0))
```

```python
import jax
import jax.numpy as jnp
from jax import lax
from jax.sharding import PartitionSpec as P

EPSILON = 1e-05


def layer_norm(states, norm_gain, norm_bias):
    values = states.astype(jnp.float32)
    center = jnp.mean(values, axis=1, keepdims=True)
    shifted = values - center
    variance = jnp.mean(shifted * shifted, axis=1, keepdims=True)
    return (shifted * lax.rsqrt(variance + EPSILON) * norm_gain + norm_bias).astype(jnp.bfloat16)


def contract_last(left, right):
    return lax.dot_general(
        left, right, (((1,), (1,)), ((), ())), preferred_element_type=jnp.float32
    )


def body(states, norm_gain, norm_bias, head_table, seq_lengths, scored_index, targets, slot_mask):
    local_rows = states.shape[0]
    devices = lax.axis_size("tensor")
    position = lax.axis_index("tensor")
    first_row = position * local_rows
    scored_count = scored_index.shape[0]
    owned_count = scored_count // devices
    offset = position * owned_count
    width = states.shape[1]

    row_iota = jnp.arange(local_rows, dtype=jnp.int32)
    picker = (scored_index[:, None] - first_row == row_iota[None, :]).astype(jnp.bfloat16)
    picked = jnp.dot(picker, states, preferred_element_type=jnp.float32).astype(jnp.bfloat16)
    arrived = lax.all_to_all(
        picked.reshape(devices, owned_count, width), "tensor", 0, 0, tiled=True
    )
    owned_rows = jnp.sum(arrived.astype(jnp.float32), axis=0)
    owned_normed = layer_norm(owned_rows, norm_gain, norm_bias)
    chosen = lax.all_to_all(
        jnp.broadcast_to(owned_normed[None], (devices, owned_count, width)), "tensor", 0, 0, tiled=True
    ).reshape(scored_count, width)

    logits = contract_last(chosen, lax.all_gather(head_table, "dp", axis=1, tiled=True))
    vocab_local = head_table.shape[0]
    vocab_iota = jnp.arange(vocab_local, dtype=jnp.int32)
    target_hits = (targets - position * vocab_local)[:, None] == vocab_iota[None, :]
    target_part = jnp.sum(jnp.where(target_hits, logits, 0.0), axis=1)
    local_maxima = jnp.max(logits, axis=1)
    shifted = logits - local_maxima[:, None]
    weights = jnp.exp(shifted)
    stats = jnp.stack(
        [local_maxima, jnp.sum(weights, axis=1), jnp.sum(weights * shifted, axis=1), target_part], axis=1
    )
    gathered = lax.all_to_all(stats.reshape(devices, owned_count, 4), "tensor", 0, 0, tiled=True)
    part_max = gathered[:, :, 0]
    maxima = jnp.max(part_max, axis=0)
    gap = part_max - maxima[None, :]
    scale = jnp.exp(gap)
    totals = jnp.sum(scale * gathered[:, :, 1], axis=0)
    weighted = jnp.sum(scale * (gathered[:, :, 2] + gap * gathered[:, :, 1]), axis=0)
    target_logit = jnp.sum(gathered[:, :, 3], axis=0)

    own_index = lax.dynamic_slice_in_dim(scored_index, offset, owned_count)
    own_mask = lax.dynamic_slice_in_dim(slot_mask, offset, owned_count)
    segment = local_rows * devices // seq_lengths.shape[0]
    sequence = own_index // segment
    seq_iota = jnp.arange(seq_lengths.shape[0], dtype=jnp.int32)
    length_of = jnp.sum(
        jnp.where(sequence[:, None] == seq_iota[None, :], seq_lengths[None, :], 0), axis=1
    )
    live_slot = (own_mask == 1) & (own_index % segment < length_of)
    log_total = jnp.log(totals)
    logprob = jnp.where(live_slot, target_logit - maxima - log_total, 0.0)
    entropy = jnp.where(live_slot, log_total - weighted / totals, 0.0)
    return logprob, entropy


def solution(mesh):
    return jax.shard_map(
        body,
        mesh=mesh,
        in_specs=(
            P(("dp", "tensor"), None),
            P(),
            P(),
            P("tensor", "dp"),
            P("dp"),
            P("dp"),
            P("dp"),
            P("dp"),
        ),
        out_specs=(P(("dp", "tensor")), P(("dp", "tensor"))),
        check_vma=False,
    )
```

```python
import jax
import jax.numpy as jnp
from jax import lax
from jax.sharding import Mesh, PartitionSpec as P

EPSILON = 1e-05
TENSOR = ("tz", "ty")


def layer_norm(states, norm_gain, norm_bias):
    values = states.astype(jnp.float32)
    center = jnp.mean(values, axis=1, keepdims=True)
    shifted = values - center
    variance = jnp.mean(shifted * shifted, axis=1, keepdims=True)
    return (shifted * lax.rsqrt(variance + EPSILON) * norm_gain + norm_bias).astype(jnp.bfloat16)


def contract_last(left, right):
    return lax.dot_general(
        left, right, (((1,), (1,)), ((), ())), preferred_element_type=jnp.float32
    )


def body(states, norm_gain, norm_bias, head_table, seq_lengths, scored_index, targets, slot_mask):
    local_rows = states.shape[0]
    devices = lax.axis_size(TENSOR)
    position = lax.axis_index(TENSOR)
    first_row = position * local_rows
    scored_count = scored_index.shape[0]
    owned_count = scored_count // devices
    offset = position * owned_count
    width = states.shape[1]

    row_iota = jnp.arange(local_rows, dtype=jnp.int32)
    picker = (scored_index[:, None] - first_row == row_iota[None, :]).astype(jnp.bfloat16)
    picked = jnp.dot(picker, states, preferred_element_type=jnp.float32).astype(jnp.bfloat16)
    ring = lax.axis_size("ty")
    by_y = picked.reshape(devices // ring, ring, owned_count, width).transpose(1, 0, 2, 3)
    near = lax.all_to_all(by_y, "ty", 0, 0, tiled=True)
    near = jnp.sum(near.astype(jnp.float32), axis=0).astype(jnp.bfloat16)
    arrived = lax.all_to_all(near, "tz", 0, 0, tiled=True)
    owned_rows = jnp.sum(arrived.astype(jnp.float32), axis=0)
    owned_normed = layer_norm(owned_rows, norm_gain, norm_bias)
    chosen = lax.all_to_all(
        jnp.broadcast_to(owned_normed[None], (devices, owned_count, width)), TENSOR, 0, 0, tiled=True
    ).reshape(scored_count, width)

    logits = contract_last(chosen, lax.all_gather(head_table, "dp", axis=1, tiled=True))
    vocab_local = head_table.shape[0]
    vocab_iota = jnp.arange(vocab_local, dtype=jnp.int32)
    target_hits = (targets - position * vocab_local)[:, None] == vocab_iota[None, :]
    target_part = jnp.sum(jnp.where(target_hits, logits, 0.0), axis=1)
    local_maxima = jnp.max(logits, axis=1)
    shifted = logits - local_maxima[:, None]
    weights = jnp.exp(shifted)
    stats = jnp.stack(
        [local_maxima, jnp.sum(weights, axis=1), jnp.sum(weights * shifted, axis=1), target_part], axis=1
    )
    gathered = lax.all_to_all(stats.reshape(devices, owned_count, 4), TENSOR, 0, 0, tiled=True)
    part_max = gathered[:, :, 0]
    maxima = jnp.max(part_max, axis=0)
    gap = part_max - maxima[None, :]
    scale = jnp.exp(gap)
    totals = jnp.sum(scale * gathered[:, :, 1], axis=0)
    weighted = jnp.sum(scale * (gathered[:, :, 2] + gap * gathered[:, :, 1]), axis=0)
    target_logit = jnp.sum(gathered[:, :, 3], axis=0)

    own_index = lax.dynamic_slice_in_dim(scored_index, offset, owned_count)
    own_mask = lax.dynamic_slice_in_dim(slot_mask, offset, owned_count)
    segment = local_rows * devices // seq_lengths.shape[0]
    sequence = own_index // segment
    seq_iota = jnp.arange(seq_lengths.shape[0], dtype=jnp.int32)
    length_of = jnp.sum(
        jnp.where(sequence[:, None] == seq_iota[None, :], seq_lengths[None, :], 0), axis=1
    )
    live_slot = (own_mask == 1) & (own_index % segment < length_of)
    log_total = jnp.log(totals)
    logprob = jnp.where(live_slot, target_logit - maxima - log_total, 0.0)
    entropy = jnp.where(live_slot, log_total - weighted / totals, 0.0)
    return logprob, entropy


def split_mesh(mesh):
    grid = mesh.devices
    first = grid[0]
    coords = [getattr(d, "coords", None) for d in first]
    ring = len({c[1] for c in coords}) if all(c is not None for c in coords) else 1
    return Mesh(grid.reshape(grid.shape[0], grid.shape[1] // ring, ring), ("dp", "tz", "ty"))


def solution(mesh):
    return jax.shard_map(
        body,
        mesh=split_mesh(mesh),
        in_specs=(
            P(("dp", "tz", "ty"), None),
            P(),
            P(),
            P(("tz", "ty"), "dp"),
            P("dp"),
            P("dp"),
            P("dp"),
            P("dp"),
        ),
        out_specs=(P(("dp", "tz", "ty")), P(("dp", "tz", "ty"))),
        check_vma=False,
    )
```

```python
import jax
import jax.numpy as jnp
from jax import lax
from jax.sharding import Mesh, PartitionSpec as P

EPSILON = 1e-05
TENSOR = ("tz", "ty")


def layer_norm(states, norm_gain, norm_bias):
    values = states.astype(jnp.float32)
    center = jnp.mean(values, axis=1, keepdims=True)
    shifted = values - center
    variance = jnp.mean(shifted * shifted, axis=1, keepdims=True)
    return (shifted * lax.rsqrt(variance + EPSILON) * norm_gain + norm_bias).astype(jnp.bfloat16)


def contract_last(left, right):
    return lax.dot_general(
        left, right, (((1,), (1,)), ((), ())), preferred_element_type=jnp.float32
    )


def body(states, norm_gain, norm_bias, head_table, seq_lengths, scored_index, targets, slot_mask):
    local_rows = states.shape[0]
    devices = lax.axis_size(TENSOR)
    position = lax.axis_index(TENSOR)
    first_row = position * local_rows
    scored_count = scored_index.shape[0]
    owned_count = scored_count // devices
    offset = position * owned_count
    width = states.shape[1]

    row_iota = jnp.arange(local_rows, dtype=jnp.int32)
    picker = (scored_index[:, None] - first_row == row_iota[None, :]).astype(jnp.bfloat16)
    picked = jnp.dot(picker, states, preferred_element_type=jnp.float32).astype(jnp.bfloat16)
    ring = lax.axis_size("ty")
    by_y = picked.reshape(devices // ring, ring, owned_count, width).transpose(1, 0, 2, 3)
    near = lax.all_to_all(by_y, "ty", 0, 0, tiled=True)
    near = jnp.sum(near.astype(jnp.float32), axis=0).astype(jnp.bfloat16)
    arrived = lax.all_to_all(near, "tz", 0, 0, tiled=True)
    owned_rows = jnp.sum(arrived.astype(jnp.float32), axis=0)
    owned_normed = layer_norm(owned_rows, norm_gain, norm_bias)
    along_z = lax.all_to_all(
        jnp.broadcast_to(owned_normed[None], (devices // ring, owned_count, width)), "tz", 0, 0, tiled=True
    )
    along_y = lax.all_to_all(
        jnp.broadcast_to(along_z[None], (ring, devices // ring, owned_count, width)), "ty", 0, 0, tiled=True
    )
    chosen = along_y.transpose(1, 0, 2, 3).reshape(scored_count, width)

    logits = contract_last(chosen, lax.all_gather(head_table, "dp", axis=1, tiled=True))
    vocab_local = head_table.shape[0]
    vocab_iota = jnp.arange(vocab_local, dtype=jnp.int32)
    target_hits = (targets - position * vocab_local)[:, None] == vocab_iota[None, :]
    target_part = jnp.sum(jnp.where(target_hits, logits, 0.0), axis=1)
    local_maxima = jnp.max(logits, axis=1)
    shifted = logits - local_maxima[:, None]
    weights = jnp.exp(shifted)
    stats = jnp.stack(
        [local_maxima, jnp.sum(weights, axis=1), jnp.sum(weights * shifted, axis=1), target_part], axis=1
    )
    gathered = lax.all_to_all(stats.reshape(devices, owned_count, 4), TENSOR, 0, 0, tiled=True)
    part_max = gathered[:, :, 0]
    maxima = jnp.max(part_max, axis=0)
    gap = part_max - maxima[None, :]
    scale = jnp.exp(gap)
    totals = jnp.sum(scale * gathered[:, :, 1], axis=0)
    weighted = jnp.sum(scale * (gathered[:, :, 2] + gap * gathered[:, :, 1]), axis=0)
    target_logit = jnp.sum(gathered[:, :, 3], axis=0)

    own_index = lax.dynamic_slice_in_dim(scored_index, offset, owned_count)
    own_mask = lax.dynamic_slice_in_dim(slot_mask, offset, owned_count)
    segment = local_rows * devices // seq_lengths.shape[0]
    sequence = own_index // segment
    seq_iota = jnp.arange(seq_lengths.shape[0], dtype=jnp.int32)
    length_of = jnp.sum(
        jnp.where(sequence[:, None] == seq_iota[None, :], seq_lengths[None, :], 0), axis=1
    )
    live_slot = (own_mask == 1) & (own_index % segment < length_of)
    log_total = jnp.log(totals)
    logprob = jnp.where(live_slot, target_logit - maxima - log_total, 0.0)
    entropy = jnp.where(live_slot, log_total - weighted / totals, 0.0)
    return logprob, entropy


def split_mesh(mesh):
    grid = mesh.devices
    first = grid[0]
    coords = [getattr(d, "coords", None) for d in first]
    ring = len({c[1] for c in coords}) if all(c is not None for c in coords) else 1
    return Mesh(grid.reshape(grid.shape[0], grid.shape[1] // ring, ring), ("dp", "tz", "ty"))


def solution(mesh):
    return jax.shard_map(
        body,
        mesh=split_mesh(mesh),
        in_specs=(
            P(("dp", "tz", "ty"), None),
            P(),
            P(),
            P(("tz", "ty"), "dp"),
            P("dp"),
            P("dp"),
            P("dp"),
            P("dp"),
        ),
        out_specs=(P(("dp", "tz", "ty")), P(("dp", "tz", "ty"))),
        check_vma=False,
    )
```

```python
import jax
import jax.numpy as jnp
from jax import lax
from jax.sharding import Mesh, PartitionSpec as P

EPSILON = 1e-05
TENSOR = ("tz", "ty")


def layer_norm(states, norm_gain, norm_bias):
    values = states.astype(jnp.float32)
    center = jnp.mean(values, axis=1, keepdims=True)
    shifted = values - center
    variance = jnp.mean(shifted * shifted, axis=1, keepdims=True)
    return (shifted * lax.rsqrt(variance + EPSILON) * norm_gain + norm_bias).astype(jnp.bfloat16)


def contract_last(left, right):
    return lax.dot_general(
        left, right, (((1,), (1,)), ((), ())), preferred_element_type=jnp.float32
    )


def body(states, norm_gain, norm_bias, head_table, seq_lengths, scored_index, targets, slot_mask):
    local_rows = states.shape[0]
    devices = lax.axis_size(TENSOR)
    position = lax.axis_index(TENSOR)
    first_row = position * local_rows
    scored_count = scored_index.shape[0]
    owned_count = scored_count // devices
    offset = position * owned_count
    width = states.shape[1]

    row_iota = jnp.arange(local_rows, dtype=jnp.int32)
    picker = (scored_index[:, None] - first_row == row_iota[None, :]).astype(jnp.bfloat16)
    picked = jnp.dot(picker, states, preferred_element_type=jnp.float32).astype(jnp.bfloat16)
    ring = lax.axis_size("ty")
    by_y = picked.reshape(devices // ring, ring, owned_count, width).transpose(1, 0, 2, 3)
    near = lax.all_to_all(by_y, "ty", 0, 0, tiled=True)
    near = jnp.sum(near.astype(jnp.float32), axis=0).astype(jnp.bfloat16)
    arrived = lax.all_to_all(near, "tz", 0, 0, tiled=True)
    owned_rows = jnp.sum(arrived.astype(jnp.float32), axis=0)
    owned_normed = layer_norm(owned_rows, norm_gain, norm_bias)
    along_z = lax.all_to_all(
        jnp.broadcast_to(owned_normed[None], (devices // ring, owned_count, width)), "tz", 0, 0, tiled=True
    )
    along_y = lax.all_to_all(
        jnp.broadcast_to(along_z[None], (ring, devices // ring, owned_count, width)), "ty", 0, 0, tiled=True
    )
    chosen = along_y.transpose(1, 0, 2, 3).reshape(scored_count, width)

    vocab_local = head_table.shape[0]
    split = (vocab_local // 32) * 16
    local_target = targets - position * vocab_local
    parts = []
    for low, high in ((0, split), (split, vocab_local)):
        logits = contract_last(chosen, lax.all_gather(head_table[low:high], "dp", axis=1, tiled=True))
        vocab_iota = jnp.arange(low, high, dtype=jnp.int32)
        target_hits = local_target[:, None] == vocab_iota[None, :]
        part_maxima = jnp.max(logits, axis=1)
        shifted = logits - part_maxima[:, None]
        weights = jnp.exp(shifted)
        parts.append(
            jnp.stack(
                [
                    part_maxima,
                    jnp.sum(weights, axis=1),
                    jnp.sum(weights * shifted, axis=1),
                    jnp.sum(jnp.where(target_hits, logits, 0.0), axis=1),
                ],
                axis=1,
            )
        )
    stats = jnp.stack(parts, axis=1)
    gathered = lax.all_to_all(stats.reshape(devices, owned_count, 2, 4), TENSOR, 0, 0, tiled=True)
    gathered = gathered.transpose(0, 2, 1, 3).reshape(devices * 2, owned_count, 4)
    part_max = gathered[:, :, 0]
    maxima = jnp.max(part_max, axis=0)
    gap = part_max - maxima[None, :]
    scale = jnp.exp(gap)
    totals = jnp.sum(scale * gathered[:, :, 1], axis=0)
    weighted = jnp.sum(scale * (gathered[:, :, 2] + gap * gathered[:, :, 1]), axis=0)
    target_logit = jnp.sum(gathered[:, :, 3], axis=0)

    own_index = lax.dynamic_slice_in_dim(scored_index, offset, owned_count)
    own_mask = lax.dynamic_slice_in_dim(slot_mask, offset, owned_count)
    segment = local_rows * devices // seq_lengths.shape[0]
    sequence = own_index // segment
    seq_iota = jnp.arange(seq_lengths.shape[0], dtype=jnp.int32)
    length_of = jnp.sum(
        jnp.where(sequence[:, None] == seq_iota[None, :], seq_lengths[None, :], 0), axis=1
    )
    live_slot = (own_mask == 1) & (own_index % segment < length_of)
    log_total = jnp.log(totals)
    logprob = jnp.where(live_slot, target_logit - maxima - log_total, 0.0)
    entropy = jnp.where(live_slot, log_total - weighted / totals, 0.0)
    return logprob, entropy


def split_mesh(mesh):
    grid = mesh.devices
    first = grid[0]
    coords = [getattr(d, "coords", None) for d in first]
    ring = len({c[1] for c in coords}) if all(c is not None for c in coords) else 1
    return Mesh(grid.reshape(grid.shape[0], grid.shape[1] // ring, ring), ("dp", "tz", "ty"))


def solution(mesh):
    return jax.shard_map(
        body,
        mesh=split_mesh(mesh),
        in_specs=(
            P(("dp", "tz", "ty"), None),
            P(),
            P(),
            P(("tz", "ty"), "dp"),
            P("dp"),
            P("dp"),
            P("dp"),
            P("dp"),
        ),
        out_specs=(P(("dp", "tz", "ty")), P(("dp", "tz", "ty"))),
        check_vma=False,
    )
```

```python
import jax
import jax.numpy as jnp
from jax import lax
from jax.sharding import Mesh, PartitionSpec as P

EPSILON = 1e-05
TENSOR = ("tz", "ty")


def layer_norm(states, norm_gain, norm_bias):
    values = states.astype(jnp.float32)
    center = jnp.mean(values, axis=1, keepdims=True)
    shifted = values - center
    variance = jnp.mean(shifted * shifted, axis=1, keepdims=True)
    return (shifted * lax.rsqrt(variance + EPSILON) * norm_gain + norm_bias).astype(jnp.bfloat16)


def contract_last(left, right):
    return lax.dot_general(
        left, right, (((1,), (1,)), ((), ())), preferred_element_type=jnp.float32
    )


def body(states, norm_gain, norm_bias, head_table, seq_lengths, scored_index, targets, slot_mask):
    local_rows = states.shape[0]
    devices = lax.axis_size(TENSOR)
    position = lax.axis_index(TENSOR)
    first_row = position * local_rows
    scored_count = scored_index.shape[0]
    owned_count = scored_count // devices
    offset = position * owned_count
    width = states.shape[1]

    row_iota = jnp.arange(local_rows, dtype=jnp.int32)
    picker = (scored_index[:, None] - first_row == row_iota[None, :]).astype(jnp.bfloat16)
    picked = jnp.dot(picker, states, preferred_element_type=jnp.float32).astype(jnp.bfloat16)
    ring = lax.axis_size("ty")
    by_y = picked.reshape(devices // ring, ring, owned_count, width).transpose(1, 0, 2, 3)
    near = lax.all_to_all(by_y, "ty", 0, 0, tiled=True)
    near = jnp.sum(near.astype(jnp.float32), axis=0).astype(jnp.bfloat16)
    arrived = lax.all_to_all(near, "tz", 0, 0, tiled=True)
    owned_rows = jnp.sum(arrived.astype(jnp.float32), axis=0)
    owned_normed = layer_norm(owned_rows, norm_gain, norm_bias)
    along_z = lax.all_to_all(
        jnp.broadcast_to(owned_normed[None], (devices // ring, owned_count, width)), "tz", 0, 0, tiled=True
    )
    along_y = lax.all_to_all(
        jnp.broadcast_to(along_z[None], (ring, devices // ring, owned_count, width)), "ty", 0, 0, tiled=True
    )
    chosen = along_y.transpose(1, 0, 2, 3).reshape(scored_count, width)

    blocks = lax.all_gather(head_table, "dp", axis=0, tiled=False)
    logits = lax.dot_general(
        chosen.reshape(scored_count, blocks.shape[0], blocks.shape[2]),
        blocks,
        (((1, 2), (0, 2)), ((), ())),
        preferred_element_type=jnp.float32,
    )
    vocab_local = head_table.shape[0]
    vocab_iota = jnp.arange(vocab_local, dtype=jnp.int32)
    target_hits = (targets - position * vocab_local)[:, None] == vocab_iota[None, :]
    target_part = jnp.sum(jnp.where(target_hits, logits, 0.0), axis=1)
    local_maxima = jnp.max(logits, axis=1)
    shifted = logits - local_maxima[:, None]
    weights = jnp.exp(shifted)
    stats = jnp.stack(
        [local_maxima, jnp.sum(weights, axis=1), jnp.sum(weights * shifted, axis=1), target_part], axis=1
    )
    gathered = lax.all_to_all(stats.reshape(devices, owned_count, 4), TENSOR, 0, 0, tiled=True)
    part_max = gathered[:, :, 0]
    maxima = jnp.max(part_max, axis=0)
    gap = part_max - maxima[None, :]
    scale = jnp.exp(gap)
    totals = jnp.sum(scale * gathered[:, :, 1], axis=0)
    weighted = jnp.sum(scale * (gathered[:, :, 2] + gap * gathered[:, :, 1]), axis=0)
    target_logit = jnp.sum(gathered[:, :, 3], axis=0)

    own_index = lax.dynamic_slice_in_dim(scored_index, offset, owned_count)
    own_mask = lax.dynamic_slice_in_dim(slot_mask, offset, owned_count)
    segment = local_rows * devices // seq_lengths.shape[0]
    sequence = own_index // segment
    seq_iota = jnp.arange(seq_lengths.shape[0], dtype=jnp.int32)
    length_of = jnp.sum(
        jnp.where(sequence[:, None] == seq_iota[None, :], seq_lengths[None, :], 0), axis=1
    )
    live_slot = (own_mask == 1) & (own_index % segment < length_of)
    log_total = jnp.log(totals)
    logprob = jnp.where(live_slot, target_logit - maxima - log_total, 0.0)
    entropy = jnp.where(live_slot, log_total - weighted / totals, 0.0)
    return logprob, entropy


def split_mesh(mesh):
    grid = mesh.devices
    first = grid[0]
    coords = [getattr(d, "coords", None) for d in first]
    ring = len({c[1] for c in coords}) if all(c is not None for c in coords) else 1
    return Mesh(grid.reshape(grid.shape[0], grid.shape[1] // ring, ring), ("dp", "tz", "ty"))


def solution(mesh):
    return jax.shard_map(
        body,
        mesh=split_mesh(mesh),
        in_specs=(
            P(("dp", "tz", "ty"), None),
            P(),
            P(),
            P(("tz", "ty"), "dp"),
            P("dp"),
            P("dp"),
            P("dp"),
            P("dp"),
        ),
        out_specs=(P(("dp", "tz", "ty")), P(("dp", "tz", "ty"))),
        check_vma=False,
    )
```

```python
import jax
import jax.numpy as jnp
from jax import lax
from jax.sharding import Mesh, PartitionSpec as P
from jax.experimental import pallas as pl
from jax.experimental.pallas import tpu as pltpu

EPSILON = 1e-05
TENSOR = ("tz", "ty")
INTERPRET = False


def layer_norm(states, norm_gain, norm_bias):
    values = states.astype(jnp.float32)
    center = jnp.mean(values, axis=1, keepdims=True)
    shifted = values - center
    variance = jnp.mean(shifted * shifted, axis=1, keepdims=True)
    return (shifted * lax.rsqrt(variance + EPSILON) * norm_gain + norm_bias).astype(jnp.bfloat16)


def contract_last(left, right):
    return lax.dot_general(
        left, right, (((1,), (1,)), ((), ())), preferred_element_type=jnp.float32
    )


def tile_of(vocab):
    best = vocab
    for size in range(8, 641, 8):
        if vocab % size == 0:
            best = size
    return best


def head_stats_kernel(chosen_ref, blocks_ref, target_ref, out_ref):
    step = pl.program_id(0)
    count, tile, part = blocks_ref.shape
    logits = jnp.zeros((tile, chosen_ref.shape[0]), jnp.float32)
    for block in range(count):
        logits = logits + lax.dot_general(
            blocks_ref[block],
            chosen_ref[:, block * part:(block + 1) * part],
            (((1,), (1,)), ((), ())),
            preferred_element_type=jnp.float32,
        )
    tile_max = jnp.max(logits, axis=0, keepdims=True)
    vocab_iota = lax.broadcasted_iota(jnp.int32, logits.shape, 0) + step * tile
    hit = jnp.sum(jnp.where(vocab_iota == target_ref[...], logits, 0.0), axis=0, keepdims=True)

    @pl.when(step == 0)
    def _():
        shifted = logits - tile_max
        weights = jnp.exp(shifted)
        out_ref[0:1, :] = tile_max
        out_ref[1:2, :] = jnp.sum(weights, axis=0, keepdims=True)
        out_ref[2:3, :] = jnp.sum(weights * shifted, axis=0, keepdims=True)
        out_ref[3:4, :] = hit

    @pl.when(step > 0)
    def _():
        old_max = out_ref[0:1, :]
        old_total = out_ref[1:2, :]
        new_max = jnp.maximum(old_max, tile_max)
        shifted = logits - new_max
        weights = jnp.exp(shifted)
        gap = old_max - new_max
        scale = jnp.exp(gap)
        out_ref[0:1, :] = new_max
        out_ref[1:2, :] = scale * old_total + jnp.sum(weights, axis=0, keepdims=True)
        out_ref[2:3, :] = scale * (out_ref[2:3, :] + gap * old_total) + jnp.sum(
            weights * shifted, axis=0, keepdims=True
        )
        out_ref[3:4, :] = out_ref[3:4, :] + hit


def head_stats(chosen, blocks, local_target):
    count, vocab, part = blocks.shape
    slots, width = chosen.shape
    tile = tile_of(vocab)
    return pl.pallas_call(
        head_stats_kernel,
        grid=(vocab // tile,),
        in_specs=[
            pl.BlockSpec((slots, width), lambda step: (0, 0)),
            pl.BlockSpec((count, tile, part), lambda step: (0, step, 0)),
            pl.BlockSpec((1, slots), lambda step: (0, 0)),
        ],
        out_specs=pl.BlockSpec((8, slots), lambda step: (0, 0)),
        out_shape=jax.ShapeDtypeStruct((8, slots), jnp.float32),
        compiler_params=pltpu.CompilerParams(dimension_semantics=("arbitrary",)),
        interpret=INTERPRET,
    )(chosen, blocks, local_target.reshape(1, slots))


def body(states, norm_gain, norm_bias, head_table, seq_lengths, scored_index, targets, slot_mask):
    local_rows = states.shape[0]
    devices = lax.axis_size(TENSOR)
    position = lax.axis_index(TENSOR)
    first_row = position * local_rows
    scored_count = scored_index.shape[0]
    owned_count = scored_count // devices
    offset = position * owned_count
    width = states.shape[1]

    row_iota = jnp.arange(local_rows, dtype=jnp.int32)
    picker = (scored_index[:, None] - first_row == row_iota[None, :]).astype(jnp.bfloat16)
    picked = jnp.dot(picker, states, preferred_element_type=jnp.float32).astype(jnp.bfloat16)
    ring = lax.axis_size("ty")
    by_y = picked.reshape(devices // ring, ring, owned_count, width).transpose(1, 0, 2, 3)
    near = lax.all_to_all(by_y, "ty", 0, 0, tiled=True)
    near = jnp.sum(near.astype(jnp.float32), axis=0).astype(jnp.bfloat16)
    arrived = lax.all_to_all(near, "tz", 0, 0, tiled=True)
    owned_rows = jnp.sum(arrived.astype(jnp.float32), axis=0)
    owned_normed = layer_norm(owned_rows, norm_gain, norm_bias)
    along_z = lax.all_to_all(
        jnp.broadcast_to(owned_normed[None], (devices // ring, owned_count, width)), "tz", 0, 0, tiled=True
    )
    along_y = lax.all_to_all(
        jnp.broadcast_to(along_z[None], (ring, devices // ring, owned_count, width)), "ty", 0, 0, tiled=True
    )
    chosen = along_y.transpose(1, 0, 2, 3).reshape(scored_count, width)

    blocks = lax.all_gather(head_table, "dp", axis=0, tiled=False)
    vocab_local = head_table.shape[0]
    stats = head_stats(chosen, blocks, targets - position * vocab_local)[:4].T
    gathered = lax.all_to_all(stats.reshape(devices, owned_count, 4), TENSOR, 0, 0, tiled=True)
    part_max = gathered[:, :, 0]
    maxima = jnp.max(part_max, axis=0)
    gap = part_max - maxima[None, :]
    scale = jnp.exp(gap)
    totals = jnp.sum(scale * gathered[:, :, 1], axis=0)
    weighted = jnp.sum(scale * (gathered[:, :, 2] + gap * gathered[:, :, 1]), axis=0)
    target_logit = jnp.sum(gathered[:, :, 3], axis=0)

    own_index = lax.dynamic_slice_in_dim(scored_index, offset, owned_count)
    own_mask = lax.dynamic_slice_in_dim(slot_mask, offset, owned_count)
    segment = local_rows * devices // seq_lengths.shape[0]
    sequence = own_index // segment
    seq_iota = jnp.arange(seq_lengths.shape[0], dtype=jnp.int32)
    length_of = jnp.sum(
        jnp.where(sequence[:, None] == seq_iota[None, :], seq_lengths[None, :], 0), axis=1
    )
    live_slot = (own_mask == 1) & (own_index % segment < length_of)
    log_total = jnp.log(totals)
    logprob = jnp.where(live_slot, target_logit - maxima - log_total, 0.0)
    entropy = jnp.where(live_slot, log_total - weighted / totals, 0.0)
    return logprob, entropy


def split_mesh(mesh):
    grid = mesh.devices
    first = grid[0]
    coords = [getattr(d, "coords", None) for d in first]
    ring = len({c[1] for c in coords}) if all(c is not None for c in coords) else 1
    return Mesh(grid.reshape(grid.shape[0], grid.shape[1] // ring, ring), ("dp", "tz", "ty"))


def solution(mesh):
    return jax.shard_map(
        body,
        mesh=split_mesh(mesh),
        in_specs=(
            P(("dp", "tz", "ty"), None),
            P(),
            P(),
            P(("tz", "ty"), "dp"),
            P("dp"),
            P("dp"),
            P("dp"),
            P("dp"),
        ),
        out_specs=(P(("dp", "tz", "ty")), P(("dp", "tz", "ty"))),
        check_vma=False,
    )
```

```python
import jax
import jax.numpy as jnp
from jax import lax
from jax.sharding import Mesh, PartitionSpec as P
from jax.experimental import pallas as pl
from jax.experimental.pallas import tpu as pltpu

EPSILON = 1e-05
TENSOR = ("tz", "ty")
INTERPRET = False


def layer_norm(states, norm_gain, norm_bias):
    values = states.astype(jnp.float32)
    center = jnp.mean(values, axis=1, keepdims=True)
    shifted = values - center
    variance = jnp.mean(shifted * shifted, axis=1, keepdims=True)
    return (shifted * lax.rsqrt(variance + EPSILON) * norm_gain + norm_bias).astype(jnp.bfloat16)


def contract_last(left, right):
    return lax.dot_general(
        left, right, (((1,), (1,)), ((), ())), preferred_element_type=jnp.float32
    )


def tile_of(vocab):
    best = vocab
    for size in range(8, 641, 8):
        if vocab % size == 0:
            best = size
    return best


def head_stats_kernel(chosen_ref, blocks_ref, target_ref, out_ref):
    step = pl.program_id(0)
    count, tile, part = blocks_ref.shape
    logits = jnp.zeros((tile, chosen_ref.shape[0]), jnp.float32)
    for block in range(count):
        logits = logits + lax.dot_general(
            blocks_ref[block],
            chosen_ref[:, block * part:(block + 1) * part],
            (((1,), (1,)), ((), ())),
            preferred_element_type=jnp.float32,
        )
    tile_max = jnp.max(logits, axis=0, keepdims=True)
    vocab_iota = lax.broadcasted_iota(jnp.int32, logits.shape, 0) + step * tile
    hit = jnp.sum(jnp.where(vocab_iota == target_ref[...], logits, 0.0), axis=0, keepdims=True)

    @pl.when(step == 0)
    def _():
        shifted = logits - tile_max
        weights = jnp.exp(shifted)
        out_ref[0:1, :] = tile_max
        out_ref[1:2, :] = jnp.sum(weights, axis=0, keepdims=True)
        out_ref[2:3, :] = jnp.sum(weights * shifted, axis=0, keepdims=True)
        out_ref[3:4, :] = hit

    @pl.when(step > 0)
    def _():
        old_max = out_ref[0:1, :]
        old_total = out_ref[1:2, :]
        new_max = jnp.maximum(old_max, tile_max)
        shifted = logits - new_max
        weights = jnp.exp(shifted)
        gap = old_max - new_max
        scale = jnp.exp(gap)
        out_ref[0:1, :] = new_max
        out_ref[1:2, :] = scale * old_total + jnp.sum(weights, axis=0, keepdims=True)
        out_ref[2:3, :] = scale * (out_ref[2:3, :] + gap * old_total) + jnp.sum(
            weights * shifted, axis=0, keepdims=True
        )
        out_ref[3:4, :] = out_ref[3:4, :] + hit


def head_stats(chosen, blocks, local_target):
    count, vocab, part = blocks.shape
    slots, width = chosen.shape
    tile = tile_of(vocab)
    return pl.pallas_call(
        head_stats_kernel,
        grid=(vocab // tile,),
        in_specs=[
            pl.BlockSpec((slots, width), lambda step: (0, 0)),
            pl.BlockSpec((count, tile, part), lambda step: (0, step, 0)),
            pl.BlockSpec((1, slots), lambda step: (0, 0)),
        ],
        out_specs=pl.BlockSpec((8, slots), lambda step: (0, 0)),
        out_shape=jax.ShapeDtypeStruct((8, slots), jnp.float32),
        compiler_params=pltpu.CompilerParams(dimension_semantics=("arbitrary",)),
        interpret=INTERPRET,
    )(chosen, blocks, local_target.reshape(1, slots))


def body(states, norm_gain, norm_bias, head_table, seq_lengths, scored_index, targets, slot_mask):
    local_rows = states.shape[0]
    devices = lax.axis_size(TENSOR)
    position = lax.axis_index(TENSOR)
    first_row = position * local_rows
    scored_count = scored_index.shape[0]
    owned_count = scored_count // devices
    offset = position * owned_count
    width = states.shape[1]

    row_iota = jnp.arange(local_rows, dtype=jnp.int32)
    picker = (scored_index[:, None] - first_row == row_iota[None, :]).astype(jnp.bfloat16)
    picked = jnp.dot(picker, states, preferred_element_type=jnp.float32).astype(jnp.bfloat16)
    ring = lax.axis_size("ty")
    by_y = picked.reshape(devices // ring, ring, owned_count, width).transpose(1, 0, 2, 3)
    near = lax.all_to_all(by_y, "ty", 0, 0, tiled=True)
    near = jnp.sum(near.astype(jnp.float32), axis=0).astype(jnp.bfloat16)
    arrived = lax.all_to_all(near, "tz", 0, 0, tiled=True)
    owned_rows = jnp.sum(arrived.astype(jnp.float32), axis=0)
    owned_normed = layer_norm(owned_rows, norm_gain, norm_bias)
    along_z = lax.all_to_all(
        jnp.broadcast_to(owned_normed[None], (devices // ring, owned_count, width)), "tz", 0, 0, tiled=True
    )
    along_y = lax.all_to_all(
        jnp.broadcast_to(along_z[None], (ring, devices // ring, owned_count, width)), "ty", 0, 0, tiled=True
    )
    chosen = along_y.reshape(scored_count, width)

    blocks = lax.all_gather(head_table, "dp", axis=0, tiled=False)
    vocab_local = head_table.shape[0]
    rings = devices // ring
    local_target = (targets - position * vocab_local).reshape(rings, ring, owned_count).transpose(1, 0, 2)
    stats = head_stats(chosen, blocks, local_target.reshape(scored_count))[:4]
    stats = stats.reshape(4, ring, rings, owned_count).transpose(2, 1, 3, 0)
    gathered = lax.all_to_all(stats.reshape(devices, owned_count, 4), TENSOR, 0, 0, tiled=True)
    part_max = gathered[:, :, 0]
    maxima = jnp.max(part_max, axis=0)
    gap = part_max - maxima[None, :]
    scale = jnp.exp(gap)
    totals = jnp.sum(scale * gathered[:, :, 1], axis=0)
    weighted = jnp.sum(scale * (gathered[:, :, 2] + gap * gathered[:, :, 1]), axis=0)
    target_logit = jnp.sum(gathered[:, :, 3], axis=0)

    own_index = lax.dynamic_slice_in_dim(scored_index, offset, owned_count)
    own_mask = lax.dynamic_slice_in_dim(slot_mask, offset, owned_count)
    segment = local_rows * devices // seq_lengths.shape[0]
    sequence = own_index // segment
    seq_iota = jnp.arange(seq_lengths.shape[0], dtype=jnp.int32)
    length_of = jnp.sum(
        jnp.where(sequence[:, None] == seq_iota[None, :], seq_lengths[None, :], 0), axis=1
    )
    live_slot = (own_mask == 1) & (own_index % segment < length_of)
    log_total = jnp.log(totals)
    logprob = jnp.where(live_slot, target_logit - maxima - log_total, 0.0)
    entropy = jnp.where(live_slot, log_total - weighted / totals, 0.0)
    return logprob, entropy


def split_mesh(mesh):
    grid = mesh.devices
    first = grid[0]
    coords = [getattr(d, "coords", None) for d in first]
    ring = len({c[1] for c in coords}) if all(c is not None for c in coords) else 1
    return Mesh(grid.reshape(grid.shape[0], grid.shape[1] // ring, ring), ("dp", "tz", "ty"))


def solution(mesh):
    return jax.shard_map(
        body,
        mesh=split_mesh(mesh),
        in_specs=(
            P(("dp", "tz", "ty"), None),
            P(),
            P(),
            P(("tz", "ty"), "dp"),
            P("dp"),
            P("dp"),
            P("dp"),
            P("dp"),
        ),
        out_specs=(P(("dp", "tz", "ty")), P(("dp", "tz", "ty"))),
        check_vma=False,
    )
```

```python
import jax
import jax.numpy as jnp
from jax import lax
from jax.sharding import Mesh, PartitionSpec as P
from jax.experimental import pallas as pl
from jax.experimental.pallas import tpu as pltpu

EPSILON = 1e-05
TENSOR = ("tz", "ty")
INTERPRET = False


def layer_norm(states, norm_gain, norm_bias):
    values = states.astype(jnp.float32)
    center = jnp.mean(values, axis=1, keepdims=True)
    shifted = values - center
    variance = jnp.mean(shifted * shifted, axis=1, keepdims=True)
    return (shifted * lax.rsqrt(variance + EPSILON) * norm_gain + norm_bias).astype(jnp.bfloat16)


def contract_last(left, right):
    return lax.dot_general(
        left, right, (((1,), (1,)), ((), ())), preferred_element_type=jnp.float32
    )


def tile_of(vocab):
    best = vocab
    for size in range(8, 641, 8):
        if vocab % size == 0:
            best = size
    return best


def head_stats_kernel(chosen_ref, blocks_ref, target_ref, out_ref):
    step = pl.program_id(0)
    count, tile, part = blocks_ref.shape
    logits = jnp.zeros((tile, chosen_ref.shape[0]), jnp.float32)
    for block in range(count):
        logits = logits + lax.dot_general(
            blocks_ref[block],
            chosen_ref[:, block * part:(block + 1) * part],
            (((1,), (1,)), ((), ())),
            preferred_element_type=jnp.float32,
        )
    tile_max = jnp.max(logits, axis=0, keepdims=True)
    vocab_iota = lax.broadcasted_iota(jnp.int32, logits.shape, 0) + step * tile
    hit = jnp.sum(jnp.where(vocab_iota == target_ref[...], logits, 0.0), axis=0, keepdims=True)

    @pl.when(step == 0)
    def _():
        shifted = logits - tile_max
        weights = jnp.exp(shifted)
        out_ref[0:1, :] = tile_max
        out_ref[1:2, :] = jnp.sum(weights, axis=0, keepdims=True)
        out_ref[2:3, :] = jnp.sum(weights * shifted, axis=0, keepdims=True)
        out_ref[3:4, :] = hit

    @pl.when(step > 0)
    def _():
        old_max = out_ref[0:1, :]
        old_total = out_ref[1:2, :]
        new_max = jnp.maximum(old_max, tile_max)
        shifted = logits - new_max
        weights = jnp.exp(shifted)
        gap = old_max - new_max
        scale = jnp.exp(gap)
        out_ref[0:1, :] = new_max
        out_ref[1:2, :] = scale * old_total + jnp.sum(weights, axis=0, keepdims=True)
        out_ref[2:3, :] = scale * (out_ref[2:3, :] + gap * old_total) + jnp.sum(
            weights * shifted, axis=0, keepdims=True
        )
        out_ref[3:4, :] = out_ref[3:4, :] + hit


def head_stats(chosen, blocks, local_target):
    count, vocab, part = blocks.shape
    slots, width = chosen.shape
    tile = tile_of(vocab)
    return pl.pallas_call(
        head_stats_kernel,
        grid=(vocab // tile,),
        in_specs=[
            pl.BlockSpec((slots, width), lambda step: (0, 0)),
            pl.BlockSpec((count, tile, part), lambda step: (0, step, 0)),
            pl.BlockSpec((1, slots), lambda step: (0, 0)),
        ],
        out_specs=pl.BlockSpec((8, slots), lambda step: (0, 0)),
        out_shape=jax.ShapeDtypeStruct((8, slots), jnp.float32),
        compiler_params=pltpu.CompilerParams(dimension_semantics=("arbitrary",)),
        interpret=INTERPRET,
    )(chosen, blocks, local_target.reshape(1, slots))


def body(states, norm_gain, norm_bias, head_table, seq_lengths, scored_index, targets, slot_mask):
    local_rows = states.shape[0]
    devices = lax.axis_size(TENSOR)
    position = lax.axis_index(TENSOR)
    first_row = position * local_rows
    scored_count = scored_index.shape[0]
    owned_count = scored_count // devices
    offset = position * owned_count
    width = states.shape[1]

    row_iota = jnp.arange(local_rows, dtype=jnp.int32)
    picker = (scored_index[:, None] - first_row == row_iota[None, :]).astype(jnp.bfloat16)
    picked = jnp.dot(picker, states, preferred_element_type=jnp.float32).astype(jnp.bfloat16)
    ring = lax.axis_size("ty")
    by_y = picked.reshape(devices // ring, ring, owned_count, width).transpose(1, 0, 2, 3)
    near = lax.all_to_all(by_y, "ty", 0, 0, tiled=True)
    near = jnp.sum(near.astype(jnp.float32), axis=0).astype(jnp.bfloat16)
    arrived = lax.all_to_all(near, "tz", 0, 0, tiled=True)
    owned_rows = jnp.sum(arrived.astype(jnp.float32), axis=0)
    owned_normed = layer_norm(owned_rows, norm_gain, norm_bias)
    along_z = lax.all_to_all(
        jnp.broadcast_to(owned_normed[None], (devices // ring, owned_count, width)), "tz", 0, 0, tiled=True
    )
    along_y = lax.all_to_all(
        jnp.broadcast_to(along_z[None], (ring, devices // ring, owned_count, width)), "ty", 0, 0, tiled=True
    )
    chosen = along_y.transpose(1, 0, 2, 3).reshape(scored_count, width)

    blocks = lax.all_gather(head_table, "dp", axis=0, tiled=False)
    vocab_local = head_table.shape[0]
    stats = head_stats(chosen, blocks, targets - position * vocab_local)[:4].T
    rings = devices // ring
    by_y = stats.reshape(rings, ring, owned_count, 4).transpose(1, 0, 2, 3)
    near = lax.all_to_all(by_y, "ty", 0, 0, tiled=True)
    gathered = lax.all_to_all(near.transpose(1, 0, 2, 3), "tz", 0, 0, tiled=True)
    gathered = gathered.reshape(devices, owned_count, 4)
    part_max = gathered[:, :, 0]
    maxima = jnp.max(part_max, axis=0)
    gap = part_max - maxima[None, :]
    scale = jnp.exp(gap)
    totals = jnp.sum(scale * gathered[:, :, 1], axis=0)
    weighted = jnp.sum(scale * (gathered[:, :, 2] + gap * gathered[:, :, 1]), axis=0)
    target_logit = jnp.sum(gathered[:, :, 3], axis=0)

    own_index = lax.dynamic_slice_in_dim(scored_index, offset, owned_count)
    own_mask = lax.dynamic_slice_in_dim(slot_mask, offset, owned_count)
    segment = local_rows * devices // seq_lengths.shape[0]
    sequence = own_index // segment
    seq_iota = jnp.arange(seq_lengths.shape[0], dtype=jnp.int32)
    length_of = jnp.sum(
        jnp.where(sequence[:, None] == seq_iota[None, :], seq_lengths[None, :], 0), axis=1
    )
    live_slot = (own_mask == 1) & (own_index % segment < length_of)
    log_total = jnp.log(totals)
    logprob = jnp.where(live_slot, target_logit - maxima - log_total, 0.0)
    entropy = jnp.where(live_slot, log_total - weighted / totals, 0.0)
    return logprob, entropy


def split_mesh(mesh):
    grid = mesh.devices
    first = grid[0]
    coords = [getattr(d, "coords", None) for d in first]
    ring = len({c[1] for c in coords}) if all(c is not None for c in coords) else 1
    return Mesh(grid.reshape(grid.shape[0], grid.shape[1] // ring, ring), ("dp", "tz", "ty"))


def solution(mesh):
    return jax.shard_map(
        body,
        mesh=split_mesh(mesh),
        in_specs=(
            P(("dp", "tz", "ty"), None),
            P(),
            P(),
            P(("tz", "ty"), "dp"),
            P("dp"),
            P("dp"),
            P("dp"),
            P("dp"),
        ),
        out_specs=(P(("dp", "tz", "ty")), P(("dp", "tz", "ty"))),
        check_vma=False,
    )
```

```python
import jax
import jax.numpy as jnp
from jax import lax
from jax.sharding import Mesh, PartitionSpec as P
from jax.experimental import pallas as pl
from jax.experimental.pallas import tpu as pltpu

EPSILON = 1e-05
TENSOR = ("tz", "ty")
INTERPRET = False


def layer_norm(states, norm_gain, norm_bias):
    values = states.astype(jnp.float32)
    center = jnp.mean(values, axis=1, keepdims=True)
    shifted = values - center
    variance = jnp.mean(shifted * shifted, axis=1, keepdims=True)
    return (shifted * lax.rsqrt(variance + EPSILON) * norm_gain + norm_bias).astype(jnp.bfloat16)


def contract_last(left, right):
    return lax.dot_general(
        left, right, (((1,), (1,)), ((), ())), preferred_element_type=jnp.float32
    )


def tile_of(vocab):
    best = vocab
    for size in range(8, 641, 8):
        if vocab % size == 0:
            best = size
    return best


def head_stats_kernel(chosen_ref, blocks_ref, target_ref, out_ref):
    step = pl.program_id(0)
    count, tile, part = blocks_ref.shape
    logits = jnp.zeros((tile, chosen_ref.shape[0]), jnp.float32)
    for block in range(count):
        logits = logits + lax.dot_general(
            blocks_ref[block],
            chosen_ref[:, block * part:(block + 1) * part],
            (((1,), (1,)), ((), ())),
            preferred_element_type=jnp.float32,
        )
    tile_max = jnp.max(logits, axis=0, keepdims=True)
    vocab_iota = lax.broadcasted_iota(jnp.int32, logits.shape, 0) + step * tile
    hit = jnp.sum(jnp.where(vocab_iota == target_ref[...], logits, 0.0), axis=0, keepdims=True)

    @pl.when(step == 0)
    def _():
        shifted = logits - tile_max
        weights = jnp.exp(shifted)
        out_ref[0:1, :] = tile_max
        out_ref[1:2, :] = jnp.sum(weights, axis=0, keepdims=True)
        out_ref[2:3, :] = jnp.sum(weights * shifted, axis=0, keepdims=True)
        out_ref[3:4, :] = hit

    @pl.when(step > 0)
    def _():
        old_max = out_ref[0:1, :]
        old_total = out_ref[1:2, :]
        new_max = jnp.maximum(old_max, tile_max)
        shifted = logits - new_max
        weights = jnp.exp(shifted)
        gap = old_max - new_max
        scale = jnp.exp(gap)
        out_ref[0:1, :] = new_max
        out_ref[1:2, :] = scale * old_total + jnp.sum(weights, axis=0, keepdims=True)
        out_ref[2:3, :] = scale * (out_ref[2:3, :] + gap * old_total) + jnp.sum(
            weights * shifted, axis=0, keepdims=True
        )
        out_ref[3:4, :] = out_ref[3:4, :] + hit


def head_stats(chosen, blocks, local_target):
    count, vocab, part = blocks.shape
    slots, width = chosen.shape
    tile = tile_of(vocab)
    return pl.pallas_call(
        head_stats_kernel,
        grid=(vocab // tile,),
        in_specs=[
            pl.BlockSpec((slots, width), lambda step: (0, 0)),
            pl.BlockSpec((count, tile, part), lambda step: (0, step, 0)),
            pl.BlockSpec((1, slots), lambda step: (0, 0)),
        ],
        out_specs=pl.BlockSpec((8, slots), lambda step: (0, 0)),
        out_shape=jax.ShapeDtypeStruct((8, slots), jnp.float32),
        compiler_params=pltpu.CompilerParams(dimension_semantics=("arbitrary",)),
        interpret=INTERPRET,
    )(chosen, blocks, local_target.reshape(1, slots))


def body(states, norm_gain, norm_bias, head_table, seq_lengths, scored_index, targets, slot_mask):
    local_rows = states.shape[0]
    devices = lax.axis_size(TENSOR)
    position = lax.axis_index(TENSOR)
    first_row = position * local_rows
    scored_count = scored_index.shape[0]
    owned_count = scored_count // devices
    offset = position * owned_count
    width = states.shape[1]

    row_iota = jnp.arange(local_rows, dtype=jnp.int32)
    picker = (scored_index[:, None] - first_row == row_iota[None, :]).astype(jnp.bfloat16)
    picked = jnp.dot(picker, states, preferred_element_type=jnp.float32).astype(jnp.bfloat16)
    ring = lax.axis_size("ty")
    by_y = picked.reshape(devices // ring, ring, owned_count, width).transpose(1, 0, 2, 3)
    near = lax.all_to_all(by_y, "ty", 0, 0, tiled=True)
    near = jnp.sum(near.astype(jnp.float32), axis=0).astype(jnp.bfloat16)
    arrived = lax.all_to_all(near, "tz", 0, 0, tiled=True)
    owned_rows = jnp.sum(arrived.astype(jnp.float32), axis=0)
    owned_normed = layer_norm(owned_rows, norm_gain, norm_bias)
    along_z = lax.all_to_all(
        jnp.broadcast_to(owned_normed[None], (devices // ring, owned_count, width)), "tz", 0, 0, tiled=True
    )
    along_y = lax.all_to_all(
        jnp.broadcast_to(along_z[None], (ring, devices // ring, owned_count, width)), "ty", 0, 0, tiled=True
    )
    chosen = along_y.transpose(1, 0, 2, 3).reshape(scored_count, width)

    blocks = lax.all_gather(head_table, "dp", axis=0, tiled=False)
    vocab_local = head_table.shape[0]
    stats = head_stats(chosen, blocks, targets - position * vocab_local)[:4].T
    gathered = lax.all_to_all(stats.reshape(devices, owned_count * 4), TENSOR, 0, 0, tiled=True)
    gathered = gathered.reshape(devices, owned_count, 4)
    part_max = gathered[:, :, 0]
    maxima = jnp.max(part_max, axis=0)
    gap = part_max - maxima[None, :]
    scale = jnp.exp(gap)
    totals = jnp.sum(scale * gathered[:, :, 1], axis=0)
    weighted = jnp.sum(scale * (gathered[:, :, 2] + gap * gathered[:, :, 1]), axis=0)
    target_logit = jnp.sum(gathered[:, :, 3], axis=0)

    own_index = lax.dynamic_slice_in_dim(scored_index, offset, owned_count)
    own_mask = lax.dynamic_slice_in_dim(slot_mask, offset, owned_count)
    segment = local_rows * devices // seq_lengths.shape[0]
    sequence = own_index // segment
    seq_iota = jnp.arange(seq_lengths.shape[0], dtype=jnp.int32)
    length_of = jnp.sum(
        jnp.where(sequence[:, None] == seq_iota[None, :], seq_lengths[None, :], 0), axis=1
    )
    live_slot = (own_mask == 1) & (own_index % segment < length_of)
    log_total = jnp.log(totals)
    logprob = jnp.where(live_slot, target_logit - maxima - log_total, 0.0)
    entropy = jnp.where(live_slot, log_total - weighted / totals, 0.0)
    return logprob, entropy


def split_mesh(mesh):
    grid = mesh.devices
    first = grid[0]
    coords = [getattr(d, "coords", None) for d in first]
    ring = len({c[1] for c in coords}) if all(c is not None for c in coords) else 1
    return Mesh(grid.reshape(grid.shape[0], grid.shape[1] // ring, ring), ("dp", "tz", "ty"))


def solution(mesh):
    return jax.shard_map(
        body,
        mesh=split_mesh(mesh),
        in_specs=(
            P(("dp", "tz", "ty"), None),
            P(),
            P(),
            P(("tz", "ty"), "dp"),
            P("dp"),
            P("dp"),
            P("dp"),
            P("dp"),
        ),
        out_specs=(P(("dp", "tz", "ty")), P(("dp", "tz", "ty"))),
        check_vma=False,
    )
```

```python
import jax
import jax.numpy as jnp
from jax import lax
from jax.sharding import Mesh, PartitionSpec as P
from jax.experimental import pallas as pl
from jax.experimental.pallas import tpu as pltpu

EPSILON = 1e-05
TENSOR = ("tz", "ty")
INTERPRET = False


def layer_norm(states, norm_gain, norm_bias):
    values = states.astype(jnp.float32)
    center = jnp.mean(values, axis=1, keepdims=True)
    shifted = values - center
    variance = jnp.mean(shifted * shifted, axis=1, keepdims=True)
    return (shifted * lax.rsqrt(variance + EPSILON) * norm_gain + norm_bias).astype(jnp.bfloat16)


def contract_last(left, right):
    return lax.dot_general(
        left, right, (((1,), (1,)), ((), ())), preferred_element_type=jnp.float32
    )


def tile_of(vocab):
    best = vocab
    for size in range(8, 801, 8):
        if vocab % size == 0:
            best = size
    return best


def head_stats_kernel(chosen_ref, blocks_ref, target_ref, out_ref):
    step = pl.program_id(0)
    count, tile, part = blocks_ref.shape
    logits = jnp.zeros((tile, chosen_ref.shape[0]), jnp.float32)
    for block in range(count):
        logits = logits + lax.dot_general(
            blocks_ref[block],
            chosen_ref[:, block * part:(block + 1) * part],
            (((1,), (1,)), ((), ())),
            preferred_element_type=jnp.float32,
        )
    tile_max = jnp.max(logits, axis=0, keepdims=True)
    vocab_iota = lax.broadcasted_iota(jnp.int32, logits.shape, 0) + step * tile
    hit = jnp.sum(jnp.where(vocab_iota == target_ref[...], logits, 0.0), axis=0, keepdims=True)

    @pl.when(step == 0)
    def _():
        shifted = logits - tile_max
        weights = jnp.exp(shifted)
        out_ref[0:1, :] = tile_max
        out_ref[1:2, :] = jnp.sum(weights, axis=0, keepdims=True)
        out_ref[2:3, :] = jnp.sum(weights * shifted, axis=0, keepdims=True)
        out_ref[3:4, :] = hit

    @pl.when(step > 0)
    def _():
        old_max = out_ref[0:1, :]
        old_total = out_ref[1:2, :]
        new_max = jnp.maximum(old_max, tile_max)
        shifted = logits - new_max
        weights = jnp.exp(shifted)
        gap = old_max - new_max
        scale = jnp.exp(gap)
        out_ref[0:1, :] = new_max
        out_ref[1:2, :] = scale * old_total + jnp.sum(weights, axis=0, keepdims=True)
        out_ref[2:3, :] = scale * (out_ref[2:3, :] + gap * old_total) + jnp.sum(
            weights * shifted, axis=0, keepdims=True
        )
        out_ref[3:4, :] = out_ref[3:4, :] + hit


def head_stats(chosen, blocks, local_target):
    count, vocab, part = blocks.shape
    slots, width = chosen.shape
    tile = tile_of(vocab)
    return pl.pallas_call(
        head_stats_kernel,
        grid=(vocab // tile,),
        in_specs=[
            pl.BlockSpec((slots, width), lambda step: (0, 0)),
            pl.BlockSpec((count, tile, part), lambda step: (0, step, 0)),
            pl.BlockSpec((1, slots), lambda step: (0, 0)),
        ],
        out_specs=pl.BlockSpec((8, slots), lambda step: (0, 0)),
        out_shape=jax.ShapeDtypeStruct((8, slots), jnp.float32),
        compiler_params=pltpu.CompilerParams(dimension_semantics=("arbitrary",)),
        interpret=INTERPRET,
    )(chosen, blocks, local_target.reshape(1, slots))


def body(states, norm_gain, norm_bias, head_table, seq_lengths, scored_index, targets, slot_mask):
    local_rows = states.shape[0]
    devices = lax.axis_size(TENSOR)
    position = lax.axis_index(TENSOR)
    first_row = position * local_rows
    scored_count = scored_index.shape[0]
    owned_count = scored_count // devices
    offset = position * owned_count
    width = states.shape[1]

    row_iota = jnp.arange(local_rows, dtype=jnp.int32)
    picker = (scored_index[:, None] - first_row == row_iota[None, :]).astype(jnp.bfloat16)
    picked = jnp.dot(picker, states, preferred_element_type=jnp.float32).astype(jnp.bfloat16)
    ring = lax.axis_size("ty")
    by_y = picked.reshape(devices // ring, ring, owned_count, width).transpose(1, 0, 2, 3)
    near = lax.all_to_all(by_y, "ty", 0, 0, tiled=True)
    near = jnp.sum(near.astype(jnp.float32), axis=0).astype(jnp.bfloat16)
    arrived = lax.all_to_all(near, "tz", 0, 0, tiled=True)
    owned_rows = jnp.sum(arrived.astype(jnp.float32), axis=0)
    owned_normed = layer_norm(owned_rows, norm_gain, norm_bias)
    along_z = lax.all_to_all(
        jnp.broadcast_to(owned_normed[None], (devices // ring, owned_count, width)), "tz", 0, 0, tiled=True
    )
    along_y = lax.all_to_all(
        jnp.broadcast_to(along_z[None], (ring, devices // ring, owned_count, width)), "ty", 0, 0, tiled=True
    )
    chosen = along_y.transpose(1, 0, 2, 3).reshape(scored_count, width)

    blocks = lax.all_gather(head_table, "dp", axis=0, tiled=False)
    vocab_local = head_table.shape[0]
    stats = head_stats(chosen, blocks, targets - position * vocab_local)[:4].T
    gathered = lax.all_to_all(stats.reshape(devices, owned_count * 4), TENSOR, 0, 0, tiled=True)
    gathered = gathered.reshape(devices, owned_count, 4)
    part_max = gathered[:, :, 0]
    maxima = jnp.max(part_max, axis=0)
    gap = part_max - maxima[None, :]
    scale = jnp.exp(gap)
    totals = jnp.sum(scale * gathered[:, :, 1], axis=0)
    weighted = jnp.sum(scale * (gathered[:, :, 2] + gap * gathered[:, :, 1]), axis=0)
    target_logit = jnp.sum(gathered[:, :, 3], axis=0)

    own_index = lax.dynamic_slice_in_dim(scored_index, offset, owned_count)
    own_mask = lax.dynamic_slice_in_dim(slot_mask, offset, owned_count)
    segment = local_rows * devices // seq_lengths.shape[0]
    sequence = own_index // segment
    seq_iota = jnp.arange(seq_lengths.shape[0], dtype=jnp.int32)
    length_of = jnp.sum(
        jnp.where(sequence[:, None] == seq_iota[None, :], seq_lengths[None, :], 0), axis=1
    )
    live_slot = (own_mask == 1) & (own_index % segment < length_of)
    log_total = jnp.log(totals)
    logprob = jnp.where(live_slot, target_logit - maxima - log_total, 0.0)
    entropy = jnp.where(live_slot, log_total - weighted / totals, 0.0)
    return logprob, entropy


def split_mesh(mesh):
    grid = mesh.devices
    first = grid[0]
    coords = [getattr(d, "coords", None) for d in first]
    ring = len({c[1] for c in coords}) if all(c is not None for c in coords) else 1
    return Mesh(grid.reshape(grid.shape[0], grid.shape[1] // ring, ring), ("dp", "tz", "ty"))


def solution(mesh):
    return jax.shard_map(
        body,
        mesh=split_mesh(mesh),
        in_specs=(
            P(("dp", "tz", "ty"), None),
            P(),
            P(),
            P(("tz", "ty"), "dp"),
            P("dp"),
            P("dp"),
            P("dp"),
            P("dp"),
        ),
        out_specs=(P(("dp", "tz", "ty")), P(("dp", "tz", "ty"))),
        check_vma=False,
    )
```

```python
import jax
import jax.numpy as jnp
from jax import lax
from jax.sharding import Mesh, PartitionSpec as P
from jax.experimental import pallas as pl
from jax.experimental.pallas import tpu as pltpu

EPSILON = 1e-05
TENSOR = ("tz", "ty")
INTERPRET = False


def layer_norm(states, norm_gain, norm_bias):
    values = states.astype(jnp.float32)
    center = jnp.mean(values, axis=1, keepdims=True)
    shifted = values - center
    variance = jnp.mean(shifted * shifted, axis=1, keepdims=True)
    return (shifted * lax.rsqrt(variance + EPSILON) * norm_gain + norm_bias).astype(jnp.bfloat16)


def contract_last(left, right):
    return lax.dot_general(
        left, right, (((1,), (1,)), ((), ())), preferred_element_type=jnp.float32
    )


def tile_of(vocab):
    best = vocab
    for size in range(8, 2001, 8):
        if vocab % size == 0:
            best = size
    return best


def head_stats_kernel(chosen_ref, blocks_ref, target_ref, out_ref):
    step = pl.program_id(0)
    count, tile, part = blocks_ref.shape
    logits = jnp.zeros((tile, chosen_ref.shape[0]), jnp.float32)
    for block in range(count):
        logits = logits + lax.dot_general(
            blocks_ref[block],
            chosen_ref[:, block * part:(block + 1) * part],
            (((1,), (1,)), ((), ())),
            preferred_element_type=jnp.float32,
        )
    tile_max = jnp.max(logits, axis=0, keepdims=True)
    vocab_iota = lax.broadcasted_iota(jnp.int32, logits.shape, 0) + step * tile
    hit = jnp.sum(jnp.where(vocab_iota == target_ref[...], logits, 0.0), axis=0, keepdims=True)

    @pl.when(step == 0)
    def _():
        shifted = logits - tile_max
        weights = jnp.exp(shifted)
        out_ref[0:1, :] = tile_max
        out_ref[1:2, :] = jnp.sum(weights, axis=0, keepdims=True)
        out_ref[2:3, :] = jnp.sum(weights * shifted, axis=0, keepdims=True)
        out_ref[3:4, :] = hit

    @pl.when(step > 0)
    def _():
        old_max = out_ref[0:1, :]
        old_total = out_ref[1:2, :]
        new_max = jnp.maximum(old_max, tile_max)
        shifted = logits - new_max
        weights = jnp.exp(shifted)
        gap = old_max - new_max
        scale = jnp.exp(gap)
        out_ref[0:1, :] = new_max
        out_ref[1:2, :] = scale * old_total + jnp.sum(weights, axis=0, keepdims=True)
        out_ref[2:3, :] = scale * (out_ref[2:3, :] + gap * old_total) + jnp.sum(
            weights * shifted, axis=0, keepdims=True
        )
        out_ref[3:4, :] = out_ref[3:4, :] + hit


def head_stats(chosen, blocks, local_target):
    count, vocab, part = blocks.shape
    slots, width = chosen.shape
    tile = tile_of(vocab)
    return pl.pallas_call(
        head_stats_kernel,
        grid=(vocab // tile,),
        in_specs=[
            pl.BlockSpec((slots, width), lambda step: (0, 0)),
            pl.BlockSpec((count, tile, part), lambda step: (0, step, 0)),
            pl.BlockSpec((1, slots), lambda step: (0, 0)),
        ],
        out_specs=pl.BlockSpec((8, slots), lambda step: (0, 0)),
        out_shape=jax.ShapeDtypeStruct((8, slots), jnp.float32),
        compiler_params=pltpu.CompilerParams(dimension_semantics=("arbitrary",)),
        interpret=INTERPRET,
    )(chosen, blocks, local_target.reshape(1, slots))


def body(states, norm_gain, norm_bias, head_table, seq_lengths, scored_index, targets, slot_mask):
    local_rows = states.shape[0]
    devices = lax.axis_size(TENSOR)
    position = lax.axis_index(TENSOR)
    first_row = position * local_rows
    scored_count = scored_index.shape[0]
    owned_count = scored_count // devices
    offset = position * owned_count
    width = states.shape[1]

    row_iota = jnp.arange(local_rows, dtype=jnp.int32)
    picker = (scored_index[:, None] - first_row == row_iota[None, :]).astype(jnp.bfloat16)
    picked = jnp.dot(picker, states, preferred_element_type=jnp.float32).astype(jnp.bfloat16)
    ring = lax.axis_size("ty")
    by_y = picked.reshape(devices // ring, ring, owned_count, width).transpose(1, 0, 2, 3)
    near = lax.all_to_all(by_y, "ty", 0, 0, tiled=True)
    near = jnp.sum(near.astype(jnp.float32), axis=0).astype(jnp.bfloat16)
    arrived = lax.all_to_all(near, "tz", 0, 0, tiled=True)
    owned_rows = jnp.sum(arrived.astype(jnp.float32), axis=0)
    owned_normed = layer_norm(owned_rows, norm_gain, norm_bias)
    along_z = lax.all_to_all(
        jnp.broadcast_to(owned_normed[None], (devices // ring, owned_count, width)), "tz", 0, 0, tiled=True
    )
    along_y = lax.all_to_all(
        jnp.broadcast_to(along_z[None], (ring, devices // ring, owned_count, width)), "ty", 0, 0, tiled=True
    )
    chosen = along_y.transpose(1, 0, 2, 3).reshape(scored_count, width)

    blocks = lax.all_gather(head_table, "dp", axis=0, tiled=False)
    vocab_local = head_table.shape[0]
    stats = head_stats(chosen, blocks, targets - position * vocab_local)[:4].T
    gathered = lax.all_to_all(stats.reshape(devices, owned_count * 4), TENSOR, 0, 0, tiled=True)
    gathered = gathered.reshape(devices, owned_count, 4)
    part_max = gathered[:, :, 0]
    maxima = jnp.max(part_max, axis=0)
    gap = part_max - maxima[None, :]
    scale = jnp.exp(gap)
    totals = jnp.sum(scale * gathered[:, :, 1], axis=0)
    weighted = jnp.sum(scale * (gathered[:, :, 2] + gap * gathered[:, :, 1]), axis=0)
    target_logit = jnp.sum(gathered[:, :, 3], axis=0)

    own_index = lax.dynamic_slice_in_dim(scored_index, offset, owned_count)
    own_mask = lax.dynamic_slice_in_dim(slot_mask, offset, owned_count)
    segment = local_rows * devices // seq_lengths.shape[0]
    sequence = own_index // segment
    seq_iota = jnp.arange(seq_lengths.shape[0], dtype=jnp.int32)
    length_of = jnp.sum(
        jnp.where(sequence[:, None] == seq_iota[None, :], seq_lengths[None, :], 0), axis=1
    )
    live_slot = (own_mask == 1) & (own_index % segment < length_of)
    log_total = jnp.log(totals)
    logprob = jnp.where(live_slot, target_logit - maxima - log_total, 0.0)
    entropy = jnp.where(live_slot, log_total - weighted / totals, 0.0)
    return logprob, entropy


def split_mesh(mesh):
    grid = mesh.devices
    first = grid[0]
    coords = [getattr(d, "coords", None) for d in first]
    ring = len({c[1] for c in coords}) if all(c is not None for c in coords) else 1
    return Mesh(grid.reshape(grid.shape[0], grid.shape[1] // ring, ring), ("dp", "tz", "ty"))


def solution(mesh):
    return jax.shard_map(
        body,
        mesh=split_mesh(mesh),
        in_specs=(
            P(("dp", "tz", "ty"), None),
            P(),
            P(),
            P(("tz", "ty"), "dp"),
            P("dp"),
            P("dp"),
            P("dp"),
            P("dp"),
        ),
        out_specs=(P(("dp", "tz", "ty")), P(("dp", "tz", "ty"))),
        check_vma=False,
    )
```

```python
import jax
import jax.numpy as jnp
from jax import lax
from jax.sharding import Mesh, PartitionSpec as P
from jax.experimental import pallas as pl
from jax.experimental.pallas import tpu as pltpu

EPSILON = 1e-05
TENSOR = ("tz", "ty")
INTERPRET = False


def layer_norm(states, norm_gain, norm_bias):
    values = states.astype(jnp.float32)
    center = jnp.mean(values, axis=1, keepdims=True)
    shifted = values - center
    variance = jnp.mean(shifted * shifted, axis=1, keepdims=True)
    return (shifted * lax.rsqrt(variance + EPSILON) * norm_gain + norm_bias).astype(jnp.bfloat16)


def contract_last(left, right):
    return lax.dot_general(
        left, right, (((1,), (1,)), ((), ())), preferred_element_type=jnp.float32
    )


def tile_of(vocab):
    best = vocab
    for size in range(8, 4001, 8):
        if vocab % size == 0:
            best = size
    return best


def head_stats_kernel(chosen_ref, blocks_ref, target_ref, out_ref):
    step = pl.program_id(0)
    count, tile, part = blocks_ref.shape
    logits = jnp.zeros((tile, chosen_ref.shape[0]), jnp.float32)
    for block in range(count):
        logits = logits + lax.dot_general(
            blocks_ref[block],
            chosen_ref[:, block * part:(block + 1) * part],
            (((1,), (1,)), ((), ())),
            preferred_element_type=jnp.float32,
        )
    tile_max = jnp.max(logits, axis=0, keepdims=True)
    vocab_iota = lax.broadcasted_iota(jnp.int32, logits.shape, 0) + step * tile
    hit = jnp.sum(jnp.where(vocab_iota == target_ref[...], logits, 0.0), axis=0, keepdims=True)

    @pl.when(step == 0)
    def _():
        shifted = logits - tile_max
        weights = jnp.exp(shifted)
        out_ref[0:1, :] = tile_max
        out_ref[1:2, :] = jnp.sum(weights, axis=0, keepdims=True)
        out_ref[2:3, :] = jnp.sum(weights * shifted, axis=0, keepdims=True)
        out_ref[3:4, :] = hit

    @pl.when(step > 0)
    def _():
        old_max = out_ref[0:1, :]
        old_total = out_ref[1:2, :]
        new_max = jnp.maximum(old_max, tile_max)
        shifted = logits - new_max
        weights = jnp.exp(shifted)
        gap = old_max - new_max
        scale = jnp.exp(gap)
        out_ref[0:1, :] = new_max
        out_ref[1:2, :] = scale * old_total + jnp.sum(weights, axis=0, keepdims=True)
        out_ref[2:3, :] = scale * (out_ref[2:3, :] + gap * old_total) + jnp.sum(
            weights * shifted, axis=0, keepdims=True
        )
        out_ref[3:4, :] = out_ref[3:4, :] + hit


def head_stats(chosen, blocks, local_target):
    count, vocab, part = blocks.shape
    slots, width = chosen.shape
    tile = tile_of(vocab)
    return pl.pallas_call(
        head_stats_kernel,
        grid=(vocab // tile,),
        in_specs=[
            pl.BlockSpec((slots, width), lambda step: (0, 0)),
            pl.BlockSpec((count, tile, part), lambda step: (0, step, 0)),
            pl.BlockSpec((1, slots), lambda step: (0, 0)),
        ],
        out_specs=pl.BlockSpec((8, slots), lambda step: (0, 0)),
        out_shape=jax.ShapeDtypeStruct((8, slots), jnp.float32),
        compiler_params=pltpu.CompilerParams(dimension_semantics=("arbitrary",)),
        interpret=INTERPRET,
    )(chosen, blocks, local_target.reshape(1, slots))


def body(states, norm_gain, norm_bias, head_table, seq_lengths, scored_index, targets, slot_mask):
    local_rows = states.shape[0]
    devices = lax.axis_size(TENSOR)
    position = lax.axis_index(TENSOR)
    first_row = position * local_rows
    scored_count = scored_index.shape[0]
    owned_count = scored_count // devices
    offset = position * owned_count
    width = states.shape[1]

    row_iota = jnp.arange(local_rows, dtype=jnp.int32)
    picker = (scored_index[:, None] - first_row == row_iota[None, :]).astype(jnp.bfloat16)
    picked = jnp.dot(picker, states, preferred_element_type=jnp.float32).astype(jnp.bfloat16)
    ring = lax.axis_size("ty")
    by_y = picked.reshape(devices // ring, ring, owned_count, width).transpose(1, 0, 2, 3)
    near = lax.all_to_all(by_y, "ty", 0, 0, tiled=True)
    near = jnp.sum(near.astype(jnp.float32), axis=0).astype(jnp.bfloat16)
    arrived = lax.all_to_all(near, "tz", 0, 0, tiled=True)
    owned_rows = jnp.sum(arrived.astype(jnp.float32), axis=0)
    owned_normed = layer_norm(owned_rows, norm_gain, norm_bias)
    along_z = lax.all_to_all(
        jnp.broadcast_to(owned_normed[None], (devices // ring, owned_count, width)), "tz", 0, 0, tiled=True
    )
    along_y = lax.all_to_all(
        jnp.broadcast_to(along_z[None], (ring, devices // ring, owned_count, width)), "ty", 0, 0, tiled=True
    )
    chosen = along_y.transpose(1, 0, 2, 3).reshape(scored_count, width)

    blocks = lax.all_gather(head_table, "dp", axis=0, tiled=False)
    vocab_local = head_table.shape[0]
    stats = head_stats(chosen, blocks, targets - position * vocab_local)[:4].T
    gathered = lax.all_to_all(stats.reshape(devices, owned_count * 4), TENSOR, 0, 0, tiled=True)
    gathered = gathered.reshape(devices, owned_count, 4)
    part_max = gathered[:, :, 0]
    maxima = jnp.max(part_max, axis=0)
    gap = part_max - maxima[None, :]
    scale = jnp.exp(gap)
    totals = jnp.sum(scale * gathered[:, :, 1], axis=0)
    weighted = jnp.sum(scale * (gathered[:, :, 2] + gap * gathered[:, :, 1]), axis=0)
    target_logit = jnp.sum(gathered[:, :, 3], axis=0)

    own_index = lax.dynamic_slice_in_dim(scored_index, offset, owned_count)
    own_mask = lax.dynamic_slice_in_dim(slot_mask, offset, owned_count)
    segment = local_rows * devices // seq_lengths.shape[0]
    sequence = own_index // segment
    seq_iota = jnp.arange(seq_lengths.shape[0], dtype=jnp.int32)
    length_of = jnp.sum(
        jnp.where(sequence[:, None] == seq_iota[None, :], seq_lengths[None, :], 0), axis=1
    )
    live_slot = (own_mask == 1) & (own_index % segment < length_of)
    log_total = jnp.log(totals)
    logprob = jnp.where(live_slot, target_logit - maxima - log_total, 0.0)
    entropy = jnp.where(live_slot, log_total - weighted / totals, 0.0)
    return logprob, entropy


def split_mesh(mesh):
    grid = mesh.devices
    first = grid[0]
    coords = [getattr(d, "coords", None) for d in first]
    ring = len({c[1] for c in coords}) if all(c is not None for c in coords) else 1
    return Mesh(grid.reshape(grid.shape[0], grid.shape[1] // ring, ring), ("dp", "tz", "ty"))


def solution(mesh):
    return jax.shard_map(
        body,
        mesh=split_mesh(mesh),
        in_specs=(
            P(("dp", "tz", "ty"), None),
            P(),
            P(),
            P(("tz", "ty"), "dp"),
            P("dp"),
            P("dp"),
            P("dp"),
            P("dp"),
        ),
        out_specs=(P(("dp", "tz", "ty")), P(("dp", "tz", "ty"))),
        check_vma=False,
    )
```
